128 devices in a mesh: req: 64 (over z, y, x), blk: 2 (over core).
Axes of the slice: x: 4, y: 4, z: 4, core: 2. Of those that a mesh axis runs over, the one named last changes fastest.
Arguments:
- normed: bfloat16 [32768, 1536], P('req', 'blk'), may hold values from -6 to 6
- router: bfloat16 [1536, 64], P('blk'), may hold values from -0.15625 to 0.15625
- adapter_down: bfloat16 [1536, 256], P('blk'), may hold values from -0.15625 to 0.15625
- adapter_up: bfloat16 [256, 1536], P(None, 'blk'), may hold values from -1.5 to 1.5
- shared_gate_up: bfloat16 [1536, 2, 1024], P(None, None, 'blk'), may hold values from -0.15625 to 0.15625
- shared_down: bfloat16 [1024, 1536], P('blk'), may hold values from -0.1875 to 0.1875
- expert_gate_up: bfloat16 [64, 1536, 1024], P('req', 'blk'), may hold values from -0.15625 to 0.15625
- expert_down: bfloat16 [64, 512, 1536], P('req', None, 'blk'), may hold values from -0.25 to 0.25
- lengths: int32 [64, 4], P('req'), may hold values from 1 to 256, 512 in all within a row
- adapter_ids: int32 [64, 4], P('req'), may hold values from 0 to 15
- routes: int32 [32768, 6], P('req'), may hold values from 0 to 63, all different within a row; in each aligned block of 512 rows (0 to 511, 512 to 1023, ...) at most 52 rows name the same one
Outputs:
- mixed: bfloat16 [32768, 1536], P('req', 'blk')
The draws below stay inside these ranges and needn't reach their ends.
Inputs may be any that keep to these rules, and one draw needn't show every extreme that they name: `lengths`: each row of an index of req lists its 4 prompts in token order; they sum to 512, the longest is 256. `routes`: each row names 6 different experts. Among the 512 rows of one index of req no expert is named more than 52 times, a bound that some block reaches.
All inputs are finite; a program needn't handle non-finite values.
Results may differ from the reference program's by a relative error of at most 0.013.
Values may be sent and summed in bfloat16 or wider, within the bound.
No kernel may reach another device: no remote copies, remote signals or barrier semaphores. Data moves between devices by JAX's collectives and lax.ppermute only.
A program may use at most 128 MiB of HBM per device.

```python
import math
import jax
import jax.numpy as jnp
import numpy as np
from jax import lax

D = 1536
FF = 512
SH = 1024
TOPK = 6
ADAPTERS = 16
RANK = 16
REQ_DEV = 4
TOK_DEV = 512
EXPERTS = 64
GROUPS = 64
TOKENS = 32768
PROMPT_MOST = 256
MOST = 52
SLOTS = 3328


def touch_ends(values, stream_key, low, largest):
    shape = values.shape
    spot = [jax.random.randint(jax.random.fold_in(stream_key, axis), (), 0, shape[axis]) for axis in range(len(shape))]
    values = values.at[tuple(spot)].set(low)
    longest = shape.index(max(shape))
    spot[longest] = (spot[longest] + 1) % shape[longest]
    return values.at[tuple(spot)].set(largest)


def level_of(key, dims, shards, smallest, top_value):
    def one(axis_at, parts):
        heights = jax.random.uniform(jax.random.fold_in(jax.random.fold_in(key, 6), axis_at), (parts,), jnp.float32, smallest / len(shards), top_value / len(shards))
        return jnp.repeat(jnp.exp(heights), dims[axis_at] // parts).reshape((-1,) + (1,) * (len(dims) - axis_at - 1))

    factor_of = one(*shards[0])
    for cut in shards[1:]:
        factor_of = factor_of * one(*cut)
    return factor_of


def profile(amount, total, most, lean):
    portions = [(1 << 20) // math.isqrt(grade ** lean) + 1 for grade in range(2, amount + 1)]
    spare, given = total - most - (amount - 1), [1] * (amount - 1)
    while spare > 0:
        movable = [i for i in range(amount - 1) if given[i] < most]
        pool, budget = sum([portions[i] for i in movable]), spare
        for i in movable:
            extra = min(most - given[i], max(1, budget * portions[i] // pool), spare)
            given[i] = given[i] + extra
            spare = spare - extra
    return np.array([most] + given)


def ragged_sizes(own_key, count, total, limit, skew):
    if count == 2:
        one = jax.random.randint(own_key, (), max(1, total - limit), min(limit, total - 1) + 1)
        return jnp.stack([one, total - one])
    sizes = jnp.asarray(profile(count, total, limit, skew), jnp.int32)
    pairs = (count - 1) // 2
    donor, taker = sizes[1:1 + 2 * pairs:2], sizes[2:2 + 2 * pairs:2]
    margin = jnp.minimum(donor - 1, limit - taker)
    passed = jax.random.randint(jax.random.fold_in(own_key, 1), (pairs,), 0, 1 << 20) % (margin + 1)
    sizes = sizes.at[1:1 + 2 * pairs:2].set(donor - passed).at[2:2 + 2 * pairs:2].set(taker + passed)
    return sizes[jax.random.permutation(jax.random.fold_in(own_key, 2), count)]


def assign_block(rng, own, number, rows, number_of, top, most, skew):
    order = jax.random.permutation(rng, number_of)
    heavy_load, usual = load_shares(number_of, rows * top, most, skew, True), load_shares(number_of, rows * top, most, skew, False)
    places = jnp.arange(number_of)

    def named(sizes, rotation):
        used = int((sizes > 0).sum())
        fixed = max(1, used // 4)
        shifted = fixed + (places - fixed + rotation * (used - fixed)) % max(1, number_of - fixed)
        return jnp.zeros((number_of,), jnp.int32).at[order[jnp.where(places < fixed, places, shifted)]].set(jnp.asarray(sizes, jnp.int32))

    sizes = jnp.where(number % 4 == 0, named(heavy_load, number // 4), named(usual, number - number // 4 - 1))
    mixed = jax.random.permutation(jax.random.fold_in(own, 3), number_of)
    donor, taker = mixed[0:number_of // 2 * 2:2], mixed[1:number_of // 2 * 2:2]
    room = jnp.minimum(sizes[donor] - 1, most - sizes[taker]) // 2
    room = jnp.where((donor == order[0]) | (taker == order[0]) | (sizes[taker] == 0), 0, jnp.maximum(room, 0))
    shifted = jax.random.randint(jax.random.fold_in(own, 4), (number_of // 2,), 0, 1 << 20) % (room + 1)
    sizes = sizes.at[donor].add(-shifted).at[taker].add(shifted)
    members = jnp.searchsorted(jnp.cumsum(sizes), jnp.arange(rows * top), side="right").astype(jnp.int32)
    table = members.reshape(top, rows).T
    table = table[jax.random.permutation(jax.random.fold_in(own, 1), rows)]
    rotation = jax.random.randint(jax.random.fold_in(own, 2), (rows, 1), 0, top)
    return jnp.take_along_axis(table, (jnp.arange(top)[None, :] + rotation) % top, axis=1)


def load_shares(amount, total, bound, skew, full):
    portions = [(1 << 20) // math.isqrt(grade ** skew) + 1 for grade in range(1, amount + 1)]
    largest = bound if full else min(bound, max(-(-total // amount), total * portions[0] // sum(portions)))
    least = 1 if total - largest >= amount - 1 else 0
    given, spare = [largest] + [least] * (amount - 1), total - largest - least * (amount - 1)
    while spare > 0:
        movable = [i for i in range(1, amount) if given[i] < largest] or [i for i in range(1, amount) if given[i] < bound]
        mass, left = sum([portions[i] for i in movable]), spare
        for i in movable:
            addition = min(bound - given[i], max(1, left * portions[i] // mass), spare)
            given[i] = given[i] + addition
            spare = spare - addition
    return np.array(given)


def gaussian(rng, dims, width, bound, cuts=(), kind=jnp.bfloat16):
    array = jax.random.normal(rng, dims, jnp.float32) * width
    if len(cuts) > 0:
        array = level_of(rng, dims, cuts, -0.22, 0.18) * array
    return jnp.clip(array, min=-bound, max=bound).astype(kind)


def setup_inputs(seed: int = 0) -> dict:
    arg_keys = jax.random.split(jax.random.key(seed), 12)
    normed = gaussian(arg_keys[0], (TOKENS, D), 1.0, 6.0, ((0, 64), (1, 2)))
    router = gaussian(arg_keys[1], (D, EXPERTS), D ** -0.5, 0.15625, ((0, 2),))
    adapter_down = gaussian(arg_keys[2], (D, ADAPTERS * RANK), D ** -0.5, 0.15625, ((0, 2),))
    adapter_up = gaussian(arg_keys[3], (ADAPTERS * RANK, D), RANK ** -0.5, 1.5, ((1, 2),))
    shared_gate_up = gaussian(arg_keys[4], (D, 2, SH), D ** -0.5, 0.15625, ((2, 2),))
    shared_down = gaussian(arg_keys[5], (SH, D), SH ** -0.5, 0.1875, ((0, 2),))
    expert_gate_up = gaussian(arg_keys[6], (EXPERTS, D, 2 * FF), D ** -0.5, 0.15625, ((0, 64), (1, 2)))
    expert_down = gaussian(arg_keys[7], (EXPERTS, FF, D), FF ** -0.5, 0.25, ((0, 64), (2, 2)))
    lengths = jax.vmap(lambda own: ragged_sizes(own, REQ_DEV, TOK_DEV, PROMPT_MOST, 2))(jax.random.split(arg_keys[8], GROUPS)).reshape((GROUPS, REQ_DEV)).astype(jnp.int32)
    adapter_ids = touch_ends(jax.random.randint(arg_keys[9], (GROUPS, REQ_DEV), 0, ADAPTERS), jax.random.fold_in(arg_keys[9], 1), 0, ADAPTERS - 1).astype(jnp.int32)
    routes_keys = jax.random.split(jax.random.fold_in(arg_keys[10], 1), TOKENS // TOK_DEV)
    routes_turns = jax.random.permutation(jax.random.fold_in(arg_keys[10], 3), TOKENS // TOK_DEV)
    routes = jax.vmap(lambda own, number: assign_block(jax.random.fold_in(arg_keys[10], 2), own, number, TOK_DEV, EXPERTS, TOPK, MOST, 1))(routes_keys, routes_turns).reshape((TOKENS, TOPK))
    return {"normed": normed, "router": router, "adapter_down": adapter_down, "adapter_up": adapter_up, "shared_gate_up": shared_gate_up, "shared_down": shared_down, "expert_gate_up": expert_gate_up, "expert_down": expert_down, "lengths": lengths, "adapter_ids": adapter_ids, "routes": routes}


def reference(normed, router, adapter_down, adapter_up, shared_gate_up, shared_down, expert_gate_up, expert_down, lengths, adapter_ids, routes):
    logits = jnp.dot(normed, router, preferred_element_type=jnp.float32)
    low_all = jnp.dot(normed, adapter_down, preferred_element_type=jnp.float32)
    ends = jnp.cumsum(lengths, axis=1).astype(jnp.int32)
    position = jnp.arange(TOK_DEV, dtype=jnp.int32)
    request = jnp.sum((position[None, :, None] >= ends[:, None, :]).astype(jnp.int32), axis=2).astype(jnp.int32)
    slots_req = jnp.arange(REQ_DEV, dtype=jnp.int32)
    adapter_token = jnp.sum(jnp.where(request[:, :, None] == slots_req[None, None, :], adapter_ids[:, None, :], 0), axis=2).astype(jnp.int32).reshape(-1)
    column_owner = jnp.arange(ADAPTERS * RANK, dtype=jnp.int32) // RANK
    low = jnp.where(column_owner[None, :] == adapter_token[:, None], low_all, 0.0).astype(jnp.bfloat16)
    delta = jnp.dot(low, adapter_up, preferred_element_type=jnp.float32)
    shared_flat = shared_gate_up.reshape(D, 2 * SH)
    shared_pre = jnp.dot(normed, shared_flat, preferred_element_type=jnp.float32)
    shared_hidden = (jax.nn.silu(shared_pre[:, :SH]) * shared_pre[:, SH:]).astype(jnp.bfloat16)
    shared_out = jnp.dot(shared_hidden, shared_down, preferred_element_type=jnp.float32)
    scores = jax.nn.sigmoid(logits)
    chosen = jnp.take_along_axis(scores, routes, axis=1)
    gate_weight = chosen / jnp.sum(chosen, axis=1, keepdims=True)

    def expert_step(total, expert):
        has_route = jnp.any(routes == expert, axis=1)
        row_index = jnp.nonzero(has_route, size=SLOTS, fill_value=0)[0].astype(jnp.int32)
        valid = jnp.arange(SLOTS, dtype=jnp.int32) < jnp.sum(has_route.astype(jnp.int32))
        picked = normed[row_index]
        gate_up = jnp.dot(picked, expert_gate_up[expert], preferred_element_type=jnp.float32)
        hidden = (jax.nn.silu(gate_up[:, :FF]) * gate_up[:, FF:]).astype(jnp.bfloat16)
        result = jnp.dot(hidden, expert_down[expert], preferred_element_type=jnp.float32).astype(jnp.bfloat16)
        result = lax.optimization_barrier(result).astype(jnp.float32)
        weight = jnp.sum(jnp.where(routes[row_index] == expert, gate_weight[row_index], 0.0), axis=1)
        weight = jnp.where(valid, weight, 0.0)
        return total.at[row_index].add(result * weight[:, None]), None

    routed, unused = lax.scan(expert_step, jnp.zeros((TOKENS, D), jnp.float32), jnp.arange(EXPERTS, dtype=jnp.int32))
    return (shared_out + 0.5 * delta + routed).astype(jnp.bfloat16)
```

```python
import jax
import jax.numpy as jnp
from jax import lax
from jax.sharding import PartitionSpec as P

RANK = 16


def body(
    normed,
    router,
    adapter_down,
    adapter_up,
    shared_gate_up,
    shared_down,
    expert_gate_up,
    expert_down,
    lengths,
    adapter_ids,
    routes,
):
    tok_rows = normed.shape[0]
    feat_local = normed.shape[1]
    top_count = routes.shape[1]
    req_count = lax.axis_size("req")
    blk_count = lax.axis_size("blk")
    expert_count = req_count * expert_gate_up.shape[0]
    most_rows = (
        tok_rows * top_count + expert_count - 1
    ) // expert_count + tok_rows * top_count // (12 * expert_count)
    part_rows = -(-most_rows // blk_count)
    most_rows = part_rows * blk_count
    hidden_width = expert_down.shape[1]

    expert_iota = jnp.arange(expert_count, dtype=jnp.int32)
    has = jnp.zeros((tok_rows, expert_count), jnp.float32)
    for k in range(top_count):
        has = has + (routes[:, k][:, None] == expert_iota[None, :]).astype(jnp.float32)
    tok_iota = jnp.arange(tok_rows, dtype=jnp.int32)
    earlier = (tok_iota[None, :] < tok_iota[:, None]).astype(jnp.bfloat16)
    rank = jnp.dot(earlier, has.astype(jnp.bfloat16), preferred_element_type=jnp.float32)
    rank = jnp.where(has > 0, rank, -1.0).astype(jnp.int32)
    slot_iota = jnp.arange(most_rows, dtype=jnp.int32)
    pick = rank.T[:, None, :] == slot_iota[None, :, None]

    send_rows = jnp.dot(
        pick.reshape(expert_count * most_rows, tok_rows).astype(jnp.bfloat16),
        normed,
        preferred_element_type=jnp.float32,
    ).astype(jnp.bfloat16)
    both = ("req", "blk")
    received = lax.all_to_all(
        send_rows.reshape(expert_count * blk_count, part_rows, feat_local),
        both,
        split_axis=0,
        concat_axis=0,
        tiled=True,
    )
    rows_in = received.reshape(req_count, blk_count, part_rows, feat_local)

    weight_gate_up = lax.all_gather(expert_gate_up[0], "blk", axis=0, tiled=True)
    weight_down = lax.all_gather(expert_down[0], "blk", axis=1, tiled=True)
    gate_up = jnp.einsum(
        "gcsd,cdf->gsf",
        rows_in,
        weight_gate_up.reshape(blk_count, feat_local, 2 * hidden_width),
        preferred_element_type=jnp.float32,
    )
    hidden = (jax.nn.silu(gate_up[..., :hidden_width]) * gate_up[..., hidden_width:]).astype(
        jnp.bfloat16
    )
    expert_out = jnp.einsum(
        "gsh,hcd->gcsd",
        hidden,
        weight_down.reshape(hidden_width, blk_count, feat_local),
        preferred_element_type=jnp.float32,
    ).astype(jnp.bfloat16)
    returned = lax.all_to_all(
        expert_out.reshape(req_count * blk_count, part_rows, feat_local),
        both,
        split_axis=0,
        concat_axis=0,
        tiled=True,
    )

    normed_full = lax.all_gather(normed, "blk", axis=1, tiled=True)
    small_w = lax.all_gather(
        jnp.concatenate([router, adapter_down], axis=1), "blk", axis=0, tiled=True
    )
    small = jnp.dot(normed_full, small_w, preferred_element_type=jnp.float32)
    logits = small[:, :expert_count]
    low_all = small[:, expert_count:]
    ends = jnp.cumsum(lengths[0])
    request = jnp.sum((tok_iota[:, None] >= ends[None, :]).astype(jnp.int32), axis=1)
    slots_req = jnp.arange(lengths.shape[1], dtype=jnp.int32)
    adapter_token = jnp.sum(
        jnp.where(request[:, None] == slots_req[None, :], adapter_ids[0][None, :], 0), axis=1
    )
    column_owner = jnp.arange(low_all.shape[1], dtype=jnp.int32) // RANK
    low = jnp.where(column_owner[None, :] == adapter_token[:, None], low_all, 0.0).astype(
        jnp.bfloat16
    )
    delta = jnp.dot(low, adapter_up, preferred_element_type=jnp.float32)
    shared_local = shared_gate_up.shape[2]
    shared_flat = shared_gate_up.reshape(shared_gate_up.shape[0], 2 * shared_local)
    shared_pre = jnp.dot(normed_full, shared_flat, preferred_element_type=jnp.float32)
    shared_hidden = (
        jax.nn.silu(shared_pre[:, :shared_local]) * shared_pre[:, shared_local:]
    ).astype(jnp.bfloat16)
    shared_terms = jnp.dot(shared_hidden, shared_down, preferred_element_type=jnp.float32)
    shared_out = lax.psum_scatter(
        shared_terms.astype(jnp.bfloat16), "blk", scatter_dimension=1, tiled=True
    ).astype(jnp.float32)

    chosen = jnp.where(has > 0, jax.nn.sigmoid(logits), 0.0)
    gate = chosen / jnp.sum(chosen, axis=1, keepdims=True)
    weights = jnp.where(pick, gate.T[:, None, :], 0.0).reshape(expert_count * most_rows, tok_rows)
    weights_hi = weights.astype(jnp.bfloat16)
    weights_lo = (weights - weights_hi.astype(jnp.float32)).astype(jnp.bfloat16)
    back = returned.reshape(expert_count * most_rows, feat_local)
    contract = (((0,), (0,)), ((), ()))
    routed = lax.dot_general(
        weights_hi, back, contract, preferred_element_type=jnp.float32
    ) + lax.dot_general(weights_lo, back, contract, preferred_element_type=jnp.float32)
    return (shared_out + 0.5 * delta + routed).astype(jnp.bfloat16)


def solution(mesh):
    return jax.shard_map(
        body,
        mesh=mesh,
        in_specs=(
            P("req", "blk"),
            P("blk", None),
            P("blk", None),
            P(None, "blk"),
            P(None, None, "blk"),
            P("blk", None),
            P("req", "blk", None),
            P("req", None, "blk"),
            P("req", None),
            P("req", None),
            P("req", None),
        ),
        out_specs=P("req", "blk"),
        check_vma=False,
    )
```

```python
import jax
import jax.numpy as jnp
from jax import lax
from jax.sharding import PartitionSpec as P

RANK = 16


def body(
    normed,
    router,
    adapter_down,
    adapter_up,
    shared_gate_up,
    shared_down,
    expert_gate_up,
    expert_down,
    lengths,
    adapter_ids,
    routes,
):
    tok_rows = normed.shape[0]
    feat_local = normed.shape[1]
    top_count = routes.shape[1]
    req_count = lax.axis_size("req")
    blk_count = lax.axis_size("blk")
    expert_count = req_count * expert_gate_up.shape[0]
    most_rows = (
        tok_rows * top_count + expert_count - 1
    ) // expert_count + tok_rows * top_count // (12 * expert_count)
    part_rows = -(-most_rows // blk_count)
    most_rows = part_rows * blk_count
    hidden_width = expert_down.shape[1]

    expert_iota = jnp.arange(expert_count, dtype=jnp.int32)
    has = jnp.zeros((tok_rows, expert_count), jnp.float32)
    for k in range(top_count):
        has = has + (routes[:, k][:, None] == expert_iota[None, :]).astype(jnp.float32)
    tok_iota = jnp.arange(tok_rows, dtype=jnp.int32)
    earlier = (tok_iota[None, :] < tok_iota[:, None]).astype(jnp.bfloat16)
    rank = jnp.dot(earlier, has.astype(jnp.bfloat16), preferred_element_type=jnp.float32)
    rank = jnp.where(has > 0, rank, -1.0).astype(jnp.int32)
    pad_rows = -(-part_rows // 16) * 16
    chunk_count = expert_count * blk_count
    row_iota = jnp.arange(chunk_count * pad_rows, dtype=jnp.int32)
    row_slot = (row_iota // pad_rows) % blk_count * part_rows + row_iota % pad_rows
    row_slot = jnp.where(row_iota % pad_rows < part_rows, row_slot, -2)
    rank_rows = jnp.broadcast_to(
        rank.T[:, None, :], (expert_count, blk_count * pad_rows, tok_rows)
    ).reshape(chunk_count * pad_rows, tok_rows)
    pick = rank_rows == row_slot[:, None]

    send_rows = jnp.dot(
        pick.astype(jnp.bfloat16), normed, preferred_element_type=jnp.float32
    ).astype(jnp.bfloat16)
    both = ("req", "blk")
    received = lax.all_to_all(
        send_rows.reshape(chunk_count, pad_rows, feat_local),
        both,
        split_axis=0,
        concat_axis=0,
        tiled=True,
    )
    rows_in = received.reshape(req_count, blk_count, pad_rows, feat_local)

    weight_gate_up = lax.all_gather(expert_gate_up[0], "blk", axis=0, tiled=True)
    weight_down = lax.all_gather(expert_down[0], "blk", axis=1, tiled=True)
    gate_up = jnp.einsum(
        "gcsd,cdf->gsf",
        rows_in,
        weight_gate_up.reshape(blk_count, feat_local, 2 * hidden_width),
        preferred_element_type=jnp.float32,
    )
    hidden = (jax.nn.silu(gate_up[..., :hidden_width]) * gate_up[..., hidden_width:]).astype(
        jnp.bfloat16
    )
    expert_out = jnp.einsum(
        "gsh,hcd->gcsd",
        hidden,
        weight_down.reshape(hidden_width, blk_count, feat_local),
        preferred_element_type=jnp.float32,
    ).astype(jnp.bfloat16)
    returned = lax.all_to_all(
        expert_out.reshape(req_count * blk_count, pad_rows, feat_local),
        both,
        split_axis=0,
        concat_axis=0,
        tiled=True,
    )

    normed_full = lax.all_gather(normed, "blk", axis=1, tiled=True)
    small_w = lax.all_gather(
        jnp.concatenate([router, adapter_down], axis=1), "blk", axis=0, tiled=True
    )
    small = jnp.dot(normed_full, small_w, preferred_element_type=jnp.float32)
    logits = small[:, :expert_count]
    low_all = small[:, expert_count:]
    ends = jnp.cumsum(lengths[0])
    request = jnp.sum((tok_iota[:, None] >= ends[None, :]).astype(jnp.int32), axis=1)
    slots_req = jnp.arange(lengths.shape[1], dtype=jnp.int32)
    adapter_token = jnp.sum(
        jnp.where(request[:, None] == slots_req[None, :], adapter_ids[0][None, :], 0), axis=1
    )
    column_owner = jnp.arange(low_all.shape[1], dtype=jnp.int32) // RANK
    low = jnp.where(column_owner[None, :] == adapter_token[:, None], low_all, 0.0).astype(
        jnp.bfloat16
    )
    delta = jnp.dot(low, adapter_up, preferred_element_type=jnp.float32)
    shared_local = shared_gate_up.shape[2]
    shared_flat = shared_gate_up.reshape(shared_gate_up.shape[0], 2 * shared_local)
    shared_pre = jnp.dot(normed_full, shared_flat, preferred_element_type=jnp.float32)
    shared_hidden = (
        jax.nn.silu(shared_pre[:, :shared_local]) * shared_pre[:, shared_local:]
    ).astype(jnp.bfloat16)
    shared_terms = jnp.dot(shared_hidden, shared_down, preferred_element_type=jnp.float32)
    shared_out = lax.psum_scatter(
        shared_terms.astype(jnp.bfloat16), "blk", scatter_dimension=1, tiled=True
    ).astype(jnp.float32)

    chosen = jnp.where(has > 0, jax.nn.sigmoid(logits), 0.0)
    gate = chosen / jnp.sum(chosen, axis=1, keepdims=True)
    gate_rows = jnp.broadcast_to(
        gate.T[:, None, :], (expert_count, blk_count * pad_rows, tok_rows)
    ).reshape(chunk_count * pad_rows, tok_rows)
    weights = jnp.where(pick, gate_rows, 0.0)
    weights_hi = weights.astype(jnp.bfloat16)
    weights_lo = (weights - weights_hi.astype(jnp.float32)).astype(jnp.bfloat16)
    back = returned.reshape(chunk_count * pad_rows, feat_local)
    contract = (((0,), (0,)), ((), ()))
    routed = lax.dot_general(
        weights_hi, back, contract, preferred_element_type=jnp.float32
    ) + lax.dot_general(weights_lo, back, contract, preferred_element_type=jnp.float32)
    return (shared_out + 0.5 * delta + routed).astype(jnp.bfloat16)


def solution(mesh):
    return jax.shard_map(
        body,
        mesh=mesh,
        in_specs=(
            P("req", "blk"),
            P("blk", None),
            P("blk", None),
            P(None, "blk"),
            P(None, None, "blk"),
            P("blk", None),
            P("req", "blk", None),
            P("req", None, "blk"),
            P("req", None),
            P("req", None),
            P("req", None),
        ),
        out_specs=P("req", "blk"),
        check_vma=False,
    )
```

```python
import jax
import jax.numpy as jnp
from jax import lax
from jax.sharding import PartitionSpec as P

RANK = 16


def body(
    normed,
    router,
    adapter_down,
    adapter_up,
    shared_gate_up,
    shared_down,
    expert_gate_up,
    expert_down,
    lengths,
    adapter_ids,
    routes,
):
    tok_rows = normed.shape[0]
    feat_local = normed.shape[1]
    top_count = routes.shape[1]
    req_count = lax.axis_size("req")
    blk_count = lax.axis_size("blk")
    expert_count = req_count * expert_gate_up.shape[0]
    most_rows = (
        tok_rows * top_count + expert_count - 1
    ) // expert_count + tok_rows * top_count // (12 * expert_count)
    part_rows = -(-most_rows // blk_count)
    most_rows = part_rows * blk_count
    hidden_width = expert_down.shape[1]

    expert_iota = jnp.arange(expert_count, dtype=jnp.int32)
    has = jnp.zeros((tok_rows, expert_count), jnp.float32)
    for k in range(top_count):
        has = has + (routes[:, k][:, None] == expert_iota[None, :]).astype(jnp.float32)
    tok_iota = jnp.arange(tok_rows, dtype=jnp.int32)
    earlier = (tok_iota[None, :] < tok_iota[:, None]).astype(jnp.bfloat16)
    rank = jnp.dot(earlier, has.astype(jnp.bfloat16), preferred_element_type=jnp.float32)
    rank = jnp.where(has > 0, rank, -1.0).astype(jnp.int32)
    wave_rows = 16
    waves = -(-part_rows // wave_rows)
    chunk_count = expert_count * blk_count
    row_iota = jnp.arange(chunk_count * wave_rows, dtype=jnp.int32)
    rank_rows = jnp.broadcast_to(
        rank.T[:, None, :], (expert_count, blk_count * wave_rows, tok_rows)
    ).reshape(chunk_count * wave_rows, tok_rows)
    both = ("req", "blk")

    def wave_pick(w):
        inner = w * wave_rows + row_iota % wave_rows
        slot = (row_iota // wave_rows) % blk_count * part_rows + inner
        slot = jnp.where(inner < part_rows, slot, -2)
        return rank_rows == slot[:, None]

    def exchange(rows):
        return lax.all_to_all(
            rows.reshape(chunk_count, wave_rows, feat_local),
            both,
            split_axis=0,
            concat_axis=0,
            tiled=True,
        )

    weight_gate_up = lax.all_gather(expert_gate_up[0], "blk", axis=0, tiled=True)
    weight_down = lax.all_gather(expert_down[0], "blk", axis=1, tiled=True)

    def expert(received):
        rows_in = received.reshape(req_count, blk_count, wave_rows, feat_local)
        gate_up = jnp.einsum(
            "gcsd,cdf->gsf",
            rows_in,
            weight_gate_up.reshape(blk_count, feat_local, 2 * hidden_width),
            preferred_element_type=jnp.float32,
        )
        hidden = (
            jax.nn.silu(gate_up[..., :hidden_width]) * gate_up[..., hidden_width:]
        ).astype(jnp.bfloat16)
        return jnp.einsum(
            "gsh,hcd->gcsd",
            hidden,
            weight_down.reshape(hidden_width, blk_count, feat_local),
            preferred_element_type=jnp.float32,
        ).astype(jnp.bfloat16)

    picks = [wave_pick(w) for w in range(waves)]
    received, last = [], None
    for w in range(waves):
        rows = jnp.dot(
            picks[w].astype(jnp.bfloat16), normed, preferred_element_type=jnp.float32
        ).astype(jnp.bfloat16)
        if last is not None:
            last, rows = lax.optimization_barrier((last, rows))
            received[-1] = last
        last = exchange(rows)
        received.append(last)
    results = [expert(r) for r in received]
    returned = []
    for w in range(waves):
        last, rows = lax.optimization_barrier((last, results[w]))
        if w > 0:
            returned[-1] = last
        last = exchange(rows)
        returned.append(last)

    normed_full = lax.all_gather(normed, "blk", axis=1, tiled=True)
    small_w = lax.all_gather(
        jnp.concatenate([router, adapter_down], axis=1), "blk", axis=0, tiled=True
    )
    small = jnp.dot(normed_full, small_w, preferred_element_type=jnp.float32)
    logits = small[:, :expert_count]
    low_all = small[:, expert_count:]
    ends = jnp.cumsum(lengths[0])
    request = jnp.sum((tok_iota[:, None] >= ends[None, :]).astype(jnp.int32), axis=1)
    slots_req = jnp.arange(lengths.shape[1], dtype=jnp.int32)
    adapter_token = jnp.sum(
        jnp.where(request[:, None] == slots_req[None, :], adapter_ids[0][None, :], 0), axis=1
    )
    column_owner = jnp.arange(low_all.shape[1], dtype=jnp.int32) // RANK
    low = jnp.where(column_owner[None, :] == adapter_token[:, None], low_all, 0.0).astype(
        jnp.bfloat16
    )
    delta = jnp.dot(low, adapter_up, preferred_element_type=jnp.float32)
    shared_local = shared_gate_up.shape[2]
    shared_flat = shared_gate_up.reshape(shared_gate_up.shape[0], 2 * shared_local)
    shared_pre = jnp.dot(normed_full, shared_flat, preferred_element_type=jnp.float32)
    shared_hidden = (
        jax.nn.silu(shared_pre[:, :shared_local]) * shared_pre[:, shared_local:]
    ).astype(jnp.bfloat16)
    shared_terms = jnp.dot(shared_hidden, shared_down, preferred_element_type=jnp.float32)
    shared_out = lax.psum_scatter(
        shared_terms.astype(jnp.bfloat16), "blk", scatter_dimension=1, tiled=True
    ).astype(jnp.float32)

    chosen = jnp.where(has > 0, jax.nn.sigmoid(logits), 0.0)
    gate = chosen / jnp.sum(chosen, axis=1, keepdims=True)
    gate_rows = jnp.broadcast_to(
        gate.T[:, None, :], (expert_count, blk_count * wave_rows, tok_rows)
    ).reshape(chunk_count * wave_rows, tok_rows)
    contract = (((0,), (0,)), ((), ()))
    routed = jnp.zeros((tok_rows, feat_local), jnp.float32)
    for w in range(waves):
        weights = jnp.where(picks[w], gate_rows, 0.0)
        weights_hi = weights.astype(jnp.bfloat16)
        weights_lo = (weights - weights_hi.astype(jnp.float32)).astype(jnp.bfloat16)
        back = returned[w].reshape(chunk_count * wave_rows, feat_local)
        routed = routed + lax.dot_general(
            weights_hi, back, contract, preferred_element_type=jnp.float32
        ) + lax.dot_general(weights_lo, back, contract, preferred_element_type=jnp.float32)
    return (shared_out + 0.5 * delta + routed).astype(jnp.bfloat16)


def solution(mesh):
    return jax.shard_map(
        body,
        mesh=mesh,
        in_specs=(
            P("req", "blk"),
            P("blk", None),
            P("blk", None),
            P(None, "blk"),
            P(None, None, "blk"),
            P("blk", None),
            P("req", "blk", None),
            P("req", None, "blk"),
            P("req", None),
            P("req", None),
            P("req", None),
        ),
        out_specs=P("req", "blk"),
        check_vma=False,
    )
```

```python
import jax
import jax.numpy as jnp
from jax import lax
from jax.sharding import PartitionSpec as P

RANK = 16


def partner(x):
    return lax.ppermute(x, "blk", [(0, 1), (1, 0)])


def gather_blk(x, axis, stack=False):
    other = partner(x)
    mine = lax.axis_index("blk")
    first = jnp.where(mine == 0, x, other)
    second = jnp.where(mine == 0, other, x)
    if stack:
        return jnp.stack([first, second], axis=axis)
    return jnp.concatenate([first, second], axis=axis)


def body(
    normed,
    router,
    adapter_down,
    adapter_up,
    shared_gate_up,
    shared_down,
    expert_gate_up,
    expert_down,
    lengths,
    adapter_ids,
    routes,
):
    tok_rows = normed.shape[0]
    feat_local = normed.shape[1]
    top_count = routes.shape[1]
    req_count = lax.axis_size("req")
    blk_count = lax.axis_size("blk")
    expert_count = req_count * expert_gate_up.shape[0]
    most_rows = (
        tok_rows * top_count + expert_count - 1
    ) // expert_count + tok_rows * top_count // (12 * expert_count)
    part_rows = -(-most_rows // blk_count)
    most_rows = part_rows * blk_count
    hidden_width = expert_down.shape[1]

    expert_iota = jnp.arange(expert_count, dtype=jnp.int32)
    has = jnp.zeros((tok_rows, expert_count), jnp.float32)
    for k in range(top_count):
        has = has + (routes[:, k][:, None] == expert_iota[None, :]).astype(jnp.float32)
    tok_iota = jnp.arange(tok_rows, dtype=jnp.int32)
    earlier = (tok_iota[None, :] < tok_iota[:, None]).astype(jnp.bfloat16)
    rank = jnp.dot(earlier, has.astype(jnp.bfloat16), preferred_element_type=jnp.float32)
    rank = jnp.where(has > 0, rank, -1.0).astype(jnp.int32)
    pad_rows = -(-part_rows // 16) * 16
    chunk_count = expert_count * blk_count
    row_iota = jnp.arange(chunk_count * pad_rows, dtype=jnp.int32)
    row_slot = (row_iota // pad_rows) % blk_count * part_rows + row_iota % pad_rows
    row_slot = jnp.where(row_iota % pad_rows < part_rows, row_slot, -2)
    rank_rows = jnp.broadcast_to(
        rank.T[:, None, :], (expert_count, blk_count * pad_rows, tok_rows)
    ).reshape(chunk_count * pad_rows, tok_rows)
    pick = rank_rows == row_slot[:, None]

    send_rows = jnp.dot(
        pick.astype(jnp.bfloat16), normed, preferred_element_type=jnp.float32
    ).astype(jnp.bfloat16)
    both = ("req", "blk")
    received = lax.all_to_all(
        send_rows.reshape(chunk_count, pad_rows, feat_local),
        both,
        split_axis=0,
        concat_axis=0,
        tiled=True,
    )
    rows_in = received.reshape(req_count, blk_count, pad_rows, feat_local)

    weight_gate_up = gather_blk(expert_gate_up[0], 0, stack=True)
    weight_down = gather_blk(expert_down[0], 1, stack=True)
    gate_up = jnp.einsum(
        "gcsd,cdf->gsf",
        rows_in,
        weight_gate_up,
        preferred_element_type=jnp.float32,
    )
    hidden = (jax.nn.silu(gate_up[..., :hidden_width]) * gate_up[..., hidden_width:]).astype(
        jnp.bfloat16
    )
    expert_out = jnp.einsum(
        "gsh,hcd->gcsd",
        hidden,
        weight_down,
        preferred_element_type=jnp.float32,
    ).astype(jnp.bfloat16)
    returned = lax.all_to_all(
        expert_out.reshape(req_count * blk_count, pad_rows, feat_local),
        both,
        split_axis=0,
        concat_axis=0,
        tiled=True,
    )

    normed_full = gather_blk(normed, 1)
    small_w = gather_blk(jnp.concatenate([router, adapter_down], axis=1), 0)
    small = jnp.dot(normed_full, small_w, preferred_element_type=jnp.float32)
    logits = small[:, :expert_count]
    low_all = small[:, expert_count:]
    ends = jnp.cumsum(lengths[0])
    request = jnp.sum((tok_iota[:, None] >= ends[None, :]).astype(jnp.int32), axis=1)
    slots_req = jnp.arange(lengths.shape[1], dtype=jnp.int32)
    adapter_token = jnp.sum(
        jnp.where(request[:, None] == slots_req[None, :], adapter_ids[0][None, :], 0), axis=1
    )
    column_owner = jnp.arange(low_all.shape[1], dtype=jnp.int32) // RANK
    low = jnp.where(column_owner[None, :] == adapter_token[:, None], low_all, 0.0).astype(
        jnp.bfloat16
    )
    delta = jnp.dot(low, adapter_up, preferred_element_type=jnp.float32)
    shared_local = shared_gate_up.shape[2]
    shared_flat = shared_gate_up.reshape(shared_gate_up.shape[0], 2 * shared_local)
    shared_pre = jnp.dot(normed_full, shared_flat, preferred_element_type=jnp.float32)
    shared_hidden = (
        jax.nn.silu(shared_pre[:, :shared_local]) * shared_pre[:, shared_local:]
    ).astype(jnp.bfloat16)
    shared_terms = jnp.dot(shared_hidden, shared_down, preferred_element_type=jnp.float32)
    terms = shared_terms.astype(jnp.bfloat16).reshape(tok_rows, blk_count, feat_local)
    mine = lax.axis_index("blk")
    keep = jnp.where(mine == 0, terms[:, 0], terms[:, 1])
    give = jnp.where(mine == 0, terms[:, 1], terms[:, 0])
    shared_out = (keep + partner(give)).astype(jnp.float32)

    chosen = jnp.where(has > 0, jax.nn.sigmoid(logits), 0.0)
    gate = chosen / jnp.sum(chosen, axis=1, keepdims=True)
    rows_per_expert = blk_count * pad_rows
    rank_cols = jnp.broadcast_to(
        rank[:, :, None], (tok_rows, expert_count, rows_per_expert)
    ).reshape(tok_rows, chunk_count * pad_rows)
    gate_cols = jnp.broadcast_to(
        gate[:, :, None], (tok_rows, expert_count, rows_per_expert)
    ).reshape(tok_rows, chunk_count * pad_rows)
    weights = jnp.where(rank_cols == row_slot[None, :], gate_cols, 0.0)
    weights_hi = weights.astype(jnp.bfloat16)
    weights_lo = (weights - weights_hi.astype(jnp.float32)).astype(jnp.bfloat16)
    back = returned.reshape(chunk_count * pad_rows, feat_local)
    routed = jnp.dot(weights_hi, back, preferred_element_type=jnp.float32) + jnp.dot(
        weights_lo, back, preferred_element_type=jnp.float32
    )
    return (shared_out + 0.5 * delta + routed).astype(jnp.bfloat16)


def solution(mesh):
    return jax.shard_map(
        body,
        mesh=mesh,
        in_specs=(
            P("req", "blk"),
            P("blk", None),
            P("blk", None),
            P(None, "blk"),
            P(None, None, "blk"),
            P("blk", None),
            P("req", "blk", None),
            P("req", None, "blk"),
            P("req", None),
            P("req", None),
            P("req", None),
        ),
        out_specs=P("req", "blk"),
        check_vma=False,
    )
```

```python
import jax
import jax.numpy as jnp
from jax import lax
from jax.sharding import PartitionSpec as P

RANK = 16


def partner(x):
    return lax.ppermute(x, "blk", [(0, 1), (1, 0)])


def gather_blk(x, axis, stack=False):
    other = partner(x)
    mine = lax.axis_index("blk")
    first = jnp.where(mine == 0, x, other)
    second = jnp.where(mine == 0, other, x)
    if stack:
        return jnp.stack([first, second], axis=axis)
    return jnp.concatenate([first, second], axis=axis)


def body(
    normed,
    router,
    adapter_down,
    adapter_up,
    shared_gate_up,
    shared_down,
    expert_gate_up,
    expert_down,
    lengths,
    adapter_ids,
    routes,
):
    tok_rows = normed.shape[0]
    feat_local = normed.shape[1]
    top_count = routes.shape[1]
    req_count = lax.axis_size("req")
    blk_count = lax.axis_size("blk")
    expert_count = req_count * expert_gate_up.shape[0]
    most_rows = (
        tok_rows * top_count + expert_count - 1
    ) // expert_count + tok_rows * top_count // (12 * expert_count)
    part_rows = -(-most_rows // blk_count)
    most_rows = part_rows * blk_count
    hidden_width = expert_down.shape[1]

    expert_iota = jnp.arange(expert_count, dtype=jnp.int32)
    has = jnp.zeros((tok_rows, expert_count), jnp.float32)
    for k in range(top_count):
        has = has + (routes[:, k][:, None] == expert_iota[None, :]).astype(jnp.float32)
    tok_iota = jnp.arange(tok_rows, dtype=jnp.int32)
    earlier = (tok_iota[None, :] < tok_iota[:, None]).astype(jnp.bfloat16)
    rank = jnp.dot(earlier, has.astype(jnp.bfloat16), preferred_element_type=jnp.float32)
    rank = jnp.where(has > 0, rank, -1.0).astype(jnp.int32)
    pad_rows = -(-part_rows // 16) * 16
    chunk_count = expert_count * blk_count
    row_iota = jnp.arange(chunk_count * pad_rows, dtype=jnp.int32)
    row_slot = (row_iota // pad_rows) % blk_count * part_rows + row_iota % pad_rows
    row_slot = jnp.where(row_iota % pad_rows < part_rows, row_slot, -2)
    rank_rows = jnp.broadcast_to(
        rank.T[:, None, :], (expert_count, blk_count * pad_rows, tok_rows)
    ).reshape(chunk_count * pad_rows, tok_rows)
    pick = rank_rows == row_slot[:, None]

    send_rows = jnp.dot(
        pick.astype(jnp.bfloat16), normed, preferred_element_type=jnp.float32
    ).astype(jnp.bfloat16)
    both = ("req", "blk")
    received = lax.all_to_all(
        send_rows.reshape(chunk_count, pad_rows, feat_local),
        both,
        split_axis=0,
        concat_axis=0,
        tiled=True,
    )
    rows_in = received.reshape(req_count, blk_count, pad_rows, feat_local)

    weight_gate_up = gather_blk(expert_gate_up[0], 0, stack=True)
    weight_down = gather_blk(expert_down[0].T, 0, stack=True)
    gate_up = jnp.einsum(
        "gcsd,cdf->gsf",
        rows_in,
        weight_gate_up,
        preferred_element_type=jnp.float32,
    )
    hidden = (jax.nn.silu(gate_up[..., :hidden_width]) * gate_up[..., hidden_width:]).astype(
        jnp.bfloat16
    )
    expert_out = jnp.einsum(
        "gsh,cdh->gcsd",
        hidden,
        weight_down,
        preferred_element_type=jnp.float32,
    ).astype(jnp.bfloat16)
    returned = lax.all_to_all(
        expert_out.reshape(req_count * blk_count, pad_rows, feat_local),
        both,
        split_axis=0,
        concat_axis=0,
        tiled=True,
    )

    send_rows, router, adapter_down, normed_late = lax.optimization_barrier(
        (send_rows, router, adapter_down, normed)
    )
    normed_full = gather_blk(normed_late, 1)
    small_w = gather_blk(jnp.concatenate([router, adapter_down], axis=1), 0)
    small = jnp.dot(normed_full, small_w, preferred_element_type=jnp.float32)
    logits = small[:, :expert_count]
    low_all = small[:, expert_count:]
    ends = jnp.cumsum(lengths[0])
    request = jnp.sum((tok_iota[:, None] >= ends[None, :]).astype(jnp.int32), axis=1)
    slots_req = jnp.arange(lengths.shape[1], dtype=jnp.int32)
    adapter_token = jnp.sum(
        jnp.where(request[:, None] == slots_req[None, :], adapter_ids[0][None, :], 0), axis=1
    )
    column_owner = jnp.arange(low_all.shape[1], dtype=jnp.int32) // RANK
    low = jnp.where(column_owner[None, :] == adapter_token[:, None], low_all, 0.0).astype(
        jnp.bfloat16
    )
    delta = jnp.dot(low, adapter_up, preferred_element_type=jnp.float32)
    shared_local = shared_gate_up.shape[2]
    shared_flat = shared_gate_up.reshape(shared_gate_up.shape[0], 2 * shared_local)
    shared_pre = jnp.dot(normed_full, shared_flat, preferred_element_type=jnp.float32)
    shared_hidden = (
        jax.nn.silu(shared_pre[:, :shared_local]) * shared_pre[:, shared_local:]
    ).astype(jnp.bfloat16)
    shared_terms = jnp.dot(shared_hidden, shared_down, preferred_element_type=jnp.float32)
    terms = shared_terms.astype(jnp.bfloat16).reshape(tok_rows, blk_count, feat_local)
    mine = lax.axis_index("blk")
    keep = jnp.where(mine == 0, terms[:, 0], terms[:, 1])
    give = jnp.where(mine == 0, terms[:, 1], terms[:, 0])
    shared_out = (keep + partner(give)).astype(jnp.float32)

    chosen = jnp.where(has > 0, jax.nn.sigmoid(logits), 0.0)
    gate = chosen / jnp.sum(chosen, axis=1, keepdims=True)
    rows_per_expert = blk_count * pad_rows
    rank_cols = jnp.broadcast_to(
        rank[:, :, None], (tok_rows, expert_count, rows_per_expert)
    ).reshape(tok_rows, chunk_count * pad_rows)
    gate_cols = jnp.broadcast_to(
        gate[:, :, None], (tok_rows, expert_count, rows_per_expert)
    ).reshape(tok_rows, chunk_count * pad_rows)
    weights = jnp.where(rank_cols == row_slot[None, :], gate_cols, 0.0)
    weights_hi = weights.astype(jnp.bfloat16)
    weights_lo = (weights - weights_hi.astype(jnp.float32)).astype(jnp.bfloat16)
    back = returned.reshape(chunk_count * pad_rows, feat_local)
    routed = jnp.dot(weights_hi, back, preferred_element_type=jnp.float32) + jnp.dot(
        weights_lo, back, preferred_element_type=jnp.float32
    )
    return (shared_out + 0.5 * delta + routed).astype(jnp.bfloat16)


def solution(mesh):
    return jax.shard_map(
        body,
        mesh=mesh,
        in_specs=(
            P("req", "blk"),
            P("blk", None),
            P("blk", None),
            P(None, "blk"),
            P(None, None, "blk"),
            P("blk", None),
            P("req", "blk", None),
            P("req", None, "blk"),
            P("req", None),
            P("req", None),
            P("req", None),
        ),
        out_specs=P("req", "blk"),
        check_vma=False,
    )
```

```python
import jax
import jax.numpy as jnp
from jax import lax
from jax.sharding import PartitionSpec as P

RANK = 16


def partner(x):
    return lax.ppermute(x, "blk", [(0, 1), (1, 0)])


def gather_blk(x, axis, stack=False):
    other = partner(x)
    mine = lax.axis_index("blk")
    first = jnp.where(mine == 0, x, other)
    second = jnp.where(mine == 0, other, x)
    if stack:
        return jnp.stack([first, second], axis=axis)
    return jnp.concatenate([first, second], axis=axis)


def body(
    normed,
    router,
    adapter_down,
    adapter_up,
    shared_gate_up,
    shared_down,
    expert_gate_up,
    expert_down,
    lengths,
    adapter_ids,
    routes,
):
    tok_rows = normed.shape[0]
    feat_local = normed.shape[1]
    top_count = routes.shape[1]
    req_count = lax.axis_size("req")
    blk_count = lax.axis_size("blk")
    expert_count = req_count * expert_gate_up.shape[0]
    most_rows = (
        tok_rows * top_count + expert_count - 1
    ) // expert_count + tok_rows * top_count // (12 * expert_count)
    part_rows = -(-most_rows // blk_count)
    most_rows = part_rows * blk_count
    hidden_width = expert_down.shape[1]

    expert_iota = jnp.arange(expert_count, dtype=jnp.int32)
    has = jnp.zeros((tok_rows, expert_count), jnp.float32)
    for k in range(top_count):
        has = has + (routes[:, k][:, None] == expert_iota[None, :]).astype(jnp.float32)
    tok_iota = jnp.arange(tok_rows, dtype=jnp.int32)
    earlier = (tok_iota[None, :] < tok_iota[:, None]).astype(jnp.bfloat16)
    rank = jnp.dot(earlier, has.astype(jnp.bfloat16), preferred_element_type=jnp.float32)
    rank = jnp.where(has > 0, rank, -1.0).astype(jnp.int32)
    pad_rows = -(-part_rows // 16) * 16
    chunk_count = expert_count * blk_count
    row_iota = jnp.arange(chunk_count * pad_rows, dtype=jnp.int32)
    row_slot = row_iota // (expert_count * pad_rows) * part_rows + row_iota % pad_rows
    row_slot = jnp.where(row_iota % pad_rows < part_rows, row_slot, -2)
    rank_rows = jnp.broadcast_to(
        rank.T[None, :, None, :], (blk_count, expert_count, pad_rows, tok_rows)
    ).reshape(chunk_count * pad_rows, tok_rows)
    pick = rank_rows == row_slot[:, None]

    send_rows = jnp.dot(
        pick.astype(jnp.bfloat16), normed, preferred_element_type=jnp.float32
    ).astype(jnp.bfloat16)
    both = ("blk", "req")
    received = lax.all_to_all(
        send_rows.reshape(chunk_count, pad_rows, feat_local),
        both,
        split_axis=0,
        concat_axis=0,
        tiled=True,
    )
    rows_in = received.reshape(blk_count, req_count, pad_rows, feat_local)

    weight_gate_up = gather_blk(expert_gate_up[0], 0, stack=True)
    weight_down = gather_blk(expert_down[0], 0, stack=True)
    gate_up = jnp.einsum(
        "cgsd,cdf->gsf",
        rows_in,
        weight_gate_up,
        preferred_element_type=jnp.float32,
    )
    hidden = (jax.nn.silu(gate_up[..., :hidden_width]) * gate_up[..., hidden_width:]).astype(
        jnp.bfloat16
    )
    hidden_rows = hidden.reshape(req_count * pad_rows, hidden_width)
    expert_out = jnp.concatenate(
        [
            jnp.dot(hidden_rows, weight_down[c], preferred_element_type=jnp.float32).astype(
                jnp.bfloat16
            )
            for c in range(blk_count)
        ],
        axis=0,
    )
    returned = lax.all_to_all(
        expert_out.reshape(req_count * blk_count, pad_rows, feat_local),
        both,
        split_axis=0,
        concat_axis=0,
        tiled=True,
    )

    send_rows, router, adapter_down, normed_late = lax.optimization_barrier(
        (send_rows, router, adapter_down, normed)
    )
    normed_full = gather_blk(normed_late, 1)
    small_w = gather_blk(jnp.concatenate([router, adapter_down], axis=1), 0)
    small = jnp.dot(normed_full, small_w, preferred_element_type=jnp.float32)
    logits = small[:, :expert_count]
    low_all = small[:, expert_count:]
    ends = jnp.cumsum(lengths[0])
    request = jnp.sum((tok_iota[:, None] >= ends[None, :]).astype(jnp.int32), axis=1)
    slots_req = jnp.arange(lengths.shape[1], dtype=jnp.int32)
    adapter_token = jnp.sum(
        jnp.where(request[:, None] == slots_req[None, :], adapter_ids[0][None, :], 0), axis=1
    )
    column_owner = jnp.arange(low_all.shape[1], dtype=jnp.int32) // RANK
    low = jnp.where(column_owner[None, :] == adapter_token[:, None], low_all, 0.0).astype(
        jnp.bfloat16
    )
    delta = jnp.dot(low, adapter_up, preferred_element_type=jnp.float32)
    shared_local = shared_gate_up.shape[2]
    shared_flat = shared_gate_up.reshape(shared_gate_up.shape[0], 2 * shared_local)
    shared_pre = jnp.dot(normed_full, shared_flat, preferred_element_type=jnp.float32)
    shared_hidden = (
        jax.nn.silu(shared_pre[:, :shared_local]) * shared_pre[:, shared_local:]
    ).astype(jnp.bfloat16)
    shared_terms = jnp.dot(shared_hidden, shared_down, preferred_element_type=jnp.float32)
    terms = shared_terms.astype(jnp.bfloat16).reshape(tok_rows, blk_count, feat_local)
    mine = lax.axis_index("blk")
    keep = jnp.where(mine == 0, terms[:, 0], terms[:, 1])
    give = jnp.where(mine == 0, terms[:, 1], terms[:, 0])
    shared_out = (keep + partner(give)).astype(jnp.float32)

    chosen = jnp.where(has > 0, jax.nn.sigmoid(logits), 0.0)
    gate = chosen / jnp.sum(chosen, axis=1, keepdims=True)
    rank_cols = jnp.broadcast_to(
        rank[:, None, :, None], (tok_rows, blk_count, expert_count, pad_rows)
    ).reshape(tok_rows, chunk_count * pad_rows)
    gate_cols = jnp.broadcast_to(
        gate[:, None, :, None], (tok_rows, blk_count, expert_count, pad_rows)
    ).reshape(tok_rows, chunk_count * pad_rows)
    weights = jnp.where(rank_cols == row_slot[None, :], gate_cols, 0.0)
    weights_hi = weights.astype(jnp.bfloat16)
    weights_lo = (weights - weights_hi.astype(jnp.float32)).astype(jnp.bfloat16)
    back = returned.reshape(chunk_count * pad_rows, feat_local)
    routed = jnp.dot(weights_hi, back, preferred_element_type=jnp.float32) + jnp.dot(
        weights_lo, back, preferred_element_type=jnp.float32
    )
    return (shared_out + 0.5 * delta + routed).astype(jnp.bfloat16)


def solution(mesh):
    return jax.shard_map(
        body,
        mesh=mesh,
        in_specs=(
            P("req", "blk"),
            P("blk", None),
            P("blk", None),
            P(None, "blk"),
            P(None, None, "blk"),
            P("blk", None),
            P("req", "blk", None),
            P("req", None, "blk"),
            P("req", None),
            P("req", None),
            P("req", None),
        ),
        out_specs=P("req", "blk"),
        check_vma=False,
    )
```

```python
import jax
import jax.numpy as jnp
from jax import lax
from jax.sharding import PartitionSpec as P

RANK = 16


def partner(x):
    return lax.ppermute(x, "blk", [(0, 1), (1, 0)])


def gather_blk(x, axis, stack=False):
    other = partner(x)
    mine = lax.axis_index("blk")
    first = jnp.where(mine == 0, x, other)
    second = jnp.where(mine == 0, other, x)
    if stack:
        return jnp.stack([first, second], axis=axis)
    return jnp.concatenate([first, second], axis=axis)


def body(
    normed,
    router,
    adapter_down,
    adapter_up,
    shared_gate_up,
    shared_down,
    expert_gate_up,
    expert_down,
    lengths,
    adapter_ids,
    routes,
):
    tok_rows = normed.shape[0]
    feat_local = normed.shape[1]
    top_count = routes.shape[1]
    req_count = lax.axis_size("req")
    blk_count = lax.axis_size("blk")
    expert_count = req_count * expert_gate_up.shape[0]
    most_rows = (
        tok_rows * top_count + expert_count - 1
    ) // expert_count + tok_rows * top_count // (12 * expert_count)
    part_rows = -(-most_rows // blk_count)
    most_rows = part_rows * blk_count
    hidden_width = expert_down.shape[1]

    expert_iota = jnp.arange(expert_count, dtype=jnp.int32)
    has = jnp.zeros((tok_rows, expert_count), jnp.float32)
    for k in range(top_count):
        has = has + (routes[:, k][:, None] == expert_iota[None, :]).astype(jnp.float32)
    tok_iota = jnp.arange(tok_rows, dtype=jnp.int32)
    earlier = (tok_iota[None, :] < tok_iota[:, None]).astype(jnp.bfloat16)
    rank = jnp.dot(earlier, has.astype(jnp.bfloat16), preferred_element_type=jnp.float32)
    rank = jnp.where(has > 0, rank, -1.0).astype(jnp.int32)
    pad_rows = -(-part_rows // 16) * 16
    chunk_count = expert_count * blk_count
    row_iota = jnp.arange(chunk_count * pad_rows, dtype=jnp.int32)
    row_slot = (row_iota // pad_rows) % blk_count * part_rows + row_iota % pad_rows
    row_slot = jnp.where(row_iota % pad_rows < part_rows, row_slot, -2)
    rank_rows = jnp.broadcast_to(
        rank.T[:, None, :], (expert_count, blk_count * pad_rows, tok_rows)
    ).reshape(chunk_count * pad_rows, tok_rows)
    pick = rank_rows == row_slot[:, None]

    send_rows = jnp.dot(
        pick.astype(jnp.bfloat16), normed, preferred_element_type=jnp.float32
    ).astype(jnp.bfloat16)
    both = ("req", "blk")
    received = lax.all_to_all(
        send_rows.reshape(chunk_count, pad_rows, feat_local),
        both,
        split_axis=0,
        concat_axis=0,
        tiled=True,
    )
    rows_in = received.reshape(req_count, blk_count, pad_rows, feat_local)

    weight_gate_up = gather_blk(expert_gate_up[0], 0, stack=True)
    gate_up = jnp.einsum(
        "gcsd,cdf->gsf",
        rows_in,
        weight_gate_up,
        preferred_element_type=jnp.float32,
    )
    hidden = (jax.nn.silu(gate_up[..., :hidden_width]) * gate_up[..., hidden_width:]).astype(
        jnp.bfloat16
    )
    hidden_rows = hidden.reshape(req_count * pad_rows, hidden_width)
    weight_down = gather_blk(expert_down[0], 0, stack=True)
    expert_out = jnp.stack(
        [
            jnp.dot(hidden_rows, weight_down[c], preferred_element_type=jnp.float32)
            .astype(jnp.bfloat16)
            .reshape(req_count, pad_rows, feat_local)
            for c in range(blk_count)
        ],
        axis=1,
    )
    returned = lax.all_to_all(
        expert_out.reshape(req_count * blk_count, pad_rows, feat_local),
        both,
        split_axis=0,
        concat_axis=0,
        tiled=True,
    )

    send_rows, router, adapter_down, normed_late = lax.optimization_barrier(
        (send_rows, router, adapter_down, normed)
    )
    normed_full = gather_blk(normed_late, 1)
    small_w = gather_blk(jnp.concatenate([router, adapter_down], axis=1), 0)
    small = jnp.dot(normed_full, small_w, preferred_element_type=jnp.float32)
    logits = small[:, :expert_count]
    low_all = small[:, expert_count:]
    ends = jnp.cumsum(lengths[0])
    request = jnp.sum((tok_iota[:, None] >= ends[None, :]).astype(jnp.int32), axis=1)
    slots_req = jnp.arange(lengths.shape[1], dtype=jnp.int32)
    adapter_token = jnp.sum(
        jnp.where(request[:, None] == slots_req[None, :], adapter_ids[0][None, :], 0), axis=1
    )
    column_owner = jnp.arange(low_all.shape[1], dtype=jnp.int32) // RANK
    low = jnp.where(column_owner[None, :] == adapter_token[:, None], low_all, 0.0).astype(
        jnp.bfloat16
    )
    delta = jnp.dot(low, adapter_up, preferred_element_type=jnp.float32)
    shared_local = shared_gate_up.shape[2]
    shared_flat = shared_gate_up.reshape(shared_gate_up.shape[0], 2 * shared_local)
    shared_pre = jnp.dot(normed_full, shared_flat, preferred_element_type=jnp.float32)
    shared_hidden = (
        jax.nn.silu(shared_pre[:, :shared_local]) * shared_pre[:, shared_local:]
    ).astype(jnp.bfloat16)
    shared_terms = jnp.dot(shared_hidden, shared_down, preferred_element_type=jnp.float32)
    terms = shared_terms.astype(jnp.bfloat16).reshape(tok_rows, blk_count, feat_local)
    mine = lax.axis_index("blk")
    keep = jnp.where(mine == 0, terms[:, 0], terms[:, 1])
    give = jnp.where(mine == 0, terms[:, 1], terms[:, 0])
    shared_out = (keep + partner(give)).astype(jnp.float32)

    chosen = jnp.where(has > 0, jax.nn.sigmoid(logits), 0.0)
    gate = chosen / jnp.sum(chosen, axis=1, keepdims=True)
    rows_per_expert = blk_count * pad_rows
    rank_cols = jnp.broadcast_to(
        rank[:, :, None], (tok_rows, expert_count, rows_per_expert)
    ).reshape(tok_rows, chunk_count * pad_rows)
    gate_cols = jnp.broadcast_to(
        gate[:, :, None], (tok_rows, expert_count, rows_per_expert)
    ).reshape(tok_rows, chunk_count * pad_rows)
    weights = jnp.where(rank_cols == row_slot[None, :], gate_cols, 0.0)
    weights_hi = weights.astype(jnp.bfloat16)
    weights_lo = (weights - weights_hi.astype(jnp.float32)).astype(jnp.bfloat16)
    back = returned.reshape(chunk_count * pad_rows, feat_local)
    routed = jnp.dot(weights_hi, back, preferred_element_type=jnp.float32) + jnp.dot(
        weights_lo, back, preferred_element_type=jnp.float32
    )
    return (shared_out + 0.5 * delta + routed).astype(jnp.bfloat16)


def solution(mesh):
    return jax.shard_map(
        body,
        mesh=mesh,
        in_specs=(
            P("req", "blk"),
            P("blk", None),
            P("blk", None),
            P(None, "blk"),
            P(None, None, "blk"),
            P("blk", None),
            P("req", "blk", None),
            P("req", None, "blk"),
            P("req", None),
            P("req", None),
            P("req", None),
        ),
        out_specs=P("req", "blk"),
        check_vma=False,
    )
```

```python
import jax
import jax.numpy as jnp
from jax import lax
from jax.sharding import PartitionSpec as P

RANK = 16


def partner(x):
    return lax.ppermute(x, "blk", [(0, 1), (1, 0)])


def gather_blk(x, axis, stack=False):
    other = partner(x)
    mine = lax.axis_index("blk")
    first = jnp.where(mine == 0, x, other)
    second = jnp.where(mine == 0, other, x)
    if stack:
        return jnp.stack([first, second], axis=axis)
    return jnp.concatenate([first, second], axis=axis)


def body(
    normed,
    router,
    adapter_down,
    adapter_up,
    shared_gate_up,
    shared_down,
    expert_gate_up,
    expert_down,
    lengths,
    adapter_ids,
    routes,
):
    tok_rows = normed.shape[0]
    feat_local = normed.shape[1]
    top_count = routes.shape[1]
    req_count = lax.axis_size("req")
    blk_count = lax.axis_size("blk")
    expert_count = req_count * expert_gate_up.shape[0]
    most_rows = (
        tok_rows * top_count + expert_count - 1
    ) // expert_count + tok_rows * top_count // (12 * expert_count)
    part_rows = -(-most_rows // blk_count)
    most_rows = part_rows * blk_count
    hidden_width = expert_down.shape[1]

    expert_iota = jnp.arange(expert_count, dtype=jnp.int32)
    has = jnp.zeros((tok_rows, expert_count), jnp.float32)
    for k in range(top_count):
        has = has + (routes[:, k][:, None] == expert_iota[None, :]).astype(jnp.float32)
    tok_iota = jnp.arange(tok_rows, dtype=jnp.int32)
    earlier = (tok_iota[None, :] < tok_iota[:, None]).astype(jnp.bfloat16)
    rank = jnp.dot(earlier, has.astype(jnp.bfloat16), preferred_element_type=jnp.float32)
    rank = jnp.where(has > 0, rank, -1.0).astype(jnp.int32)
    pad_rows = -(-part_rows // 16) * 16
    chunk_count = expert_count * blk_count
    row_iota = jnp.arange(chunk_count * pad_rows, dtype=jnp.int32)
    row_slot = (row_iota // pad_rows) % blk_count * part_rows + row_iota % pad_rows
    row_slot = jnp.where(row_iota % pad_rows < part_rows, row_slot, -2)
    rank_rows = jnp.broadcast_to(
        rank.T[:, None, :], (expert_count, blk_count * pad_rows, tok_rows)
    ).reshape(chunk_count * pad_rows, tok_rows)
    pick = rank_rows == row_slot[:, None]

    send_rows = jnp.dot(
        pick.astype(jnp.bfloat16), normed, preferred_element_type=jnp.float32
    ).astype(jnp.bfloat16)
    both = ("req", "blk")
    received = lax.all_to_all(
        send_rows.reshape(chunk_count, pad_rows, feat_local),
        both,
        split_axis=0,
        concat_axis=0,
        tiled=True,
    )
    rows_in = received.reshape(req_count, blk_count, pad_rows, feat_local)

    weight_gate_up = gather_blk(expert_gate_up[0], 0, stack=True)
    gate_up = jnp.einsum(
        "gcsd,cdf->gsf",
        rows_in,
        weight_gate_up,
        preferred_element_type=jnp.float32,
    )
    hidden = (jax.nn.silu(gate_up[..., :hidden_width]) * gate_up[..., hidden_width:]).astype(
        jnp.bfloat16
    )
    hidden_rows = hidden.reshape(req_count * pad_rows, hidden_width)
    weight_down = gather_blk(expert_down[0], 0, stack=True)
    expert_out = jnp.stack(
        [
            jnp.dot(hidden_rows, weight_down[c], preferred_element_type=jnp.float32)
            .astype(jnp.bfloat16)
            .reshape(req_count, pad_rows, feat_local)
            for c in range(blk_count)
        ],
        axis=1,
    )
    returned = lax.all_to_all(
        expert_out.reshape(req_count * blk_count, pad_rows, feat_local),
        both,
        split_axis=0,
        concat_axis=0,
        tiled=True,
    )

    send_rows, router, adapter_down, normed_late = lax.optimization_barrier(
        (send_rows, router, adapter_down, normed)
    )
    normed_full = gather_blk(normed_late, 1)
    small_w = gather_blk(jnp.concatenate([router, adapter_down], axis=1), 0)
    small = jnp.dot(normed_full, small_w, preferred_element_type=jnp.float32)
    logits = small[:, :expert_count]
    low_all = small[:, expert_count:]
    ends = jnp.cumsum(lengths[0])
    request = jnp.sum((tok_iota[:, None] >= ends[None, :]).astype(jnp.int32), axis=1)
    slots_req = jnp.arange(lengths.shape[1], dtype=jnp.int32)
    adapter_token = jnp.sum(
        jnp.where(request[:, None] == slots_req[None, :], adapter_ids[0][None, :], 0), axis=1
    )
    column_owner = jnp.arange(low_all.shape[1], dtype=jnp.int32) // RANK
    low = jnp.where(column_owner[None, :] == adapter_token[:, None], low_all, 0.0).astype(
        jnp.bfloat16
    )
    delta = jnp.dot(low, adapter_up, preferred_element_type=jnp.float32)
    shared_local = shared_gate_up.shape[2]
    shared_flat = shared_gate_up.reshape(shared_gate_up.shape[0], 2 * shared_local)
    shared_pre = jnp.dot(normed_full, shared_flat, preferred_element_type=jnp.float32)
    shared_hidden = (
        jax.nn.silu(shared_pre[:, :shared_local]) * shared_pre[:, shared_local:]
    ).astype(jnp.bfloat16)
    shared_terms = jnp.dot(shared_hidden, shared_down, preferred_element_type=jnp.float32)
    terms = shared_terms.astype(jnp.bfloat16).reshape(tok_rows, blk_count, feat_local)
    mine = lax.axis_index("blk")
    keep = jnp.where(mine == 0, terms[:, 0], terms[:, 1])
    give = jnp.where(mine == 0, terms[:, 1], terms[:, 0])
    shared_out = (keep + partner(give)).astype(jnp.float32)

    chosen = jnp.where(has > 0, jax.nn.sigmoid(logits), 0.0)
    gate = chosen / jnp.sum(chosen, axis=1, keepdims=True)
    rows_per_expert = blk_count * pad_rows
    rank_cols = jnp.broadcast_to(
        rank[:, :, None], (tok_rows, expert_count, rows_per_expert)
    ).reshape(tok_rows, chunk_count * pad_rows)
    gate_cols = jnp.broadcast_to(
        gate[:, :, None], (tok_rows, expert_count, rows_per_expert)
    ).reshape(tok_rows, chunk_count * pad_rows)
    weights = jnp.where(rank_cols == row_slot[None, :], gate_cols, 0.0)
    back = returned.reshape(chunk_count * pad_rows, feat_local)
    routed = jnp.dot(weights.astype(jnp.bfloat16), back, preferred_element_type=jnp.float32)
    return (shared_out + 0.5 * delta + routed).astype(jnp.bfloat16)


def solution(mesh):
    return jax.shard_map(
        body,
        mesh=mesh,
        in_specs=(
            P("req", "blk"),
            P("blk", None),
            P("blk", None),
            P(None, "blk"),
            P(None, None, "blk"),
            P("blk", None),
            P("req", "blk", None),
            P("req", None, "blk"),
            P("req", None),
            P("req", None),
            P("req", None),
        ),
        out_specs=P("req", "blk"),
        check_vma=False,
    )
```

```python
import jax
import jax.numpy as jnp
from jax import lax
from jax.sharding import PartitionSpec as P

RANK = 16


def partner(x):
    return lax.ppermute(x, "blk", [(0, 1), (1, 0)])


def gather_blk(x, axis, stack=False):
    other = partner(x)
    mine = lax.axis_index("blk")
    first = jnp.where(mine == 0, x, other)
    second = jnp.where(mine == 0, other, x)
    if stack:
        return jnp.stack([first, second], axis=axis)
    return jnp.concatenate([first, second], axis=axis)


def body(
    normed,
    router,
    adapter_down,
    adapter_up,
    shared_gate_up,
    shared_down,
    expert_gate_up,
    expert_down,
    lengths,
    adapter_ids,
    routes,
):
    tok_rows = normed.shape[0]
    feat_local = normed.shape[1]
    top_count = routes.shape[1]
    req_count = lax.axis_size("req")
    blk_count = lax.axis_size("blk")
    expert_count = req_count * expert_gate_up.shape[0]
    most_rows = (
        tok_rows * top_count + expert_count - 1
    ) // expert_count + tok_rows * top_count // (12 * expert_count)
    part_rows = -(-most_rows // blk_count)
    most_rows = part_rows * blk_count
    hidden_width = expert_down.shape[1]

    expert_iota = jnp.arange(expert_count, dtype=jnp.int32)
    has = jnp.zeros((tok_rows, expert_count), jnp.float32)
    for k in range(top_count):
        has = has + (routes[:, k][:, None] == expert_iota[None, :]).astype(jnp.float32)
    tok_iota = jnp.arange(tok_rows, dtype=jnp.int32)
    earlier = (tok_iota[None, :] < tok_iota[:, None]).astype(jnp.bfloat16)
    rank = jnp.dot(earlier, has.astype(jnp.bfloat16), preferred_element_type=jnp.float32)
    rank = jnp.where(has > 0, rank, -1.0).astype(jnp.int32)
    pad_rows = -(-part_rows // 16) * 16
    chunk_count = expert_count * blk_count
    row_iota = jnp.arange(chunk_count * pad_rows, dtype=jnp.int32)
    row_slot = (row_iota // pad_rows) % blk_count * part_rows + row_iota % pad_rows
    row_slot = jnp.where(row_iota % pad_rows < part_rows, row_slot, -2)
    rank_rows = jnp.broadcast_to(
        rank.T[:, None, :], (expert_count, blk_count * pad_rows, tok_rows)
    ).reshape(chunk_count * pad_rows, tok_rows)
    pick = rank_rows == row_slot[:, None]

    send_rows = jnp.dot(
        pick.astype(jnp.bfloat16), normed, preferred_element_type=jnp.float32
    ).astype(jnp.bfloat16)
    both = ("req", "blk")
    received = lax.all_to_all(
        send_rows.reshape(chunk_count, pad_rows, feat_local),
        both,
        split_axis=0,
        concat_axis=0,
        tiled=True,
    )
    rows_in = received.reshape(req_count, blk_count, pad_rows, feat_local)

    weight_gate_up = gather_blk(expert_gate_up[0], 0, stack=True)
    gate_up = jnp.einsum(
        "gcsd,cdf->gsf",
        rows_in,
        weight_gate_up,
        preferred_element_type=jnp.float32,
    )
    hidden = (jax.nn.silu(gate_up[..., :hidden_width]) * gate_up[..., hidden_width:]).astype(
        jnp.bfloat16
    )
    hidden_rows = hidden.reshape(req_count * pad_rows, hidden_width)
    weight_down = gather_blk(expert_down[0], 0, stack=True)
    expert_out = jnp.stack(
        [
            jnp.dot(hidden_rows, weight_down[c], preferred_element_type=jnp.float32)
            .astype(jnp.bfloat16)
            .reshape(req_count, pad_rows, feat_local)
            for c in range(blk_count)
        ],
        axis=1,
    )
    returned = lax.all_to_all(
        expert_out.reshape(req_count * blk_count, pad_rows, feat_local),
        both,
        split_axis=0,
        concat_axis=0,
        tiled=True,
    )

    send_rows, router, adapter_down, normed_late = lax.optimization_barrier(
        (send_rows, router, adapter_down, normed)
    )
    normed_full = gather_blk(normed_late, 1)
    small_w = gather_blk(jnp.concatenate([router, adapter_down], axis=1), 0)
    small = jnp.dot(normed_full, small_w, preferred_element_type=jnp.float32)
    logits = small[:, :expert_count]
    low_all = small[:, expert_count:]
    ends = jnp.cumsum(lengths[0])
    request = jnp.sum((tok_iota[:, None] >= ends[None, :]).astype(jnp.int32), axis=1)
    slots_req = jnp.arange(lengths.shape[1], dtype=jnp.int32)
    adapter_token = jnp.sum(
        jnp.where(request[:, None] == slots_req[None, :], adapter_ids[0][None, :], 0), axis=1
    )
    column_owner = jnp.arange(low_all.shape[1], dtype=jnp.int32) // RANK
    low = jnp.where(column_owner[None, :] == adapter_token[:, None], low_all, 0.0).astype(
        jnp.bfloat16
    )
    delta = jnp.dot(low, adapter_up, preferred_element_type=jnp.float32)
    shared_local = shared_gate_up.shape[2]
    shared_flat = shared_gate_up.reshape(shared_gate_up.shape[0], 2 * shared_local)
    shared_pre = jnp.dot(normed_full, shared_flat, preferred_element_type=jnp.float32)
    shared_hidden = (
        jax.nn.silu(shared_pre[:, :shared_local]) * shared_pre[:, shared_local:]
    ).astype(jnp.bfloat16)
    shared_terms = jnp.dot(shared_hidden, shared_down, preferred_element_type=jnp.float32)
    terms = shared_terms.astype(jnp.bfloat16).reshape(tok_rows, blk_count, feat_local)
    mine = lax.axis_index("blk")
    keep = jnp.where(mine == 0, terms[:, 0], terms[:, 1])
    give = jnp.where(mine == 0, terms[:, 1], terms[:, 0])
    shared_out = (keep + partner(give)).astype(jnp.float32)

    chosen = jnp.where(has > 0, jax.nn.sigmoid(logits), 0.0)
    gate = chosen / jnp.sum(chosen, axis=1, keepdims=True)
    rows_per_expert = blk_count * pad_rows
    rank_cols = jnp.broadcast_to(
        rank[:, :, None], (tok_rows, expert_count, rows_per_expert)
    ).reshape(tok_rows, chunk_count * pad_rows)
    gate_cols = jnp.broadcast_to(
        gate[:, :, None], (tok_rows, expert_count, rows_per_expert)
    ).reshape(tok_rows, chunk_count * pad_rows)
    weights = jnp.where(rank_cols == row_slot[None, :], gate_cols, 0.0)
    weights, base = lax.optimization_barrier(
        (weights.astype(jnp.bfloat16), shared_out + 0.5 * delta)
    )
    back = returned.reshape(chunk_count * pad_rows, feat_local)
    routed = jnp.dot(weights, back, preferred_element_type=jnp.float32)
    return (base + routed).astype(jnp.bfloat16)


def solution(mesh):
    return jax.shard_map(
        body,
        mesh=mesh,
        in_specs=(
            P("req", "blk"),
            P("blk", None),
            P("blk", None),
            P(None, "blk"),
            P(None, None, "blk"),
            P("blk", None),
            P("req", "blk", None),
            P("req", None, "blk"),
            P("req", None),
            P("req", None),
            P("req", None),
        ),
        out_specs=P("req", "blk"),
        check_vma=False,
    )
```

```python
import jax
import jax.numpy as jnp
from jax import lax
from jax.experimental.layout import Layout, with_layout_constraint
from jax.sharding import PartitionSpec as P

RANK = 16


def partner(x):
    return lax.ppermute(x, "blk", [(0, 1), (1, 0)])


def gather_blk(x, axis, stack=False):
    other = partner(x)
    mine = lax.axis_index("blk")
    first = jnp.where(mine == 0, x, other)
    second = jnp.where(mine == 0, other, x)
    if stack:
        return jnp.stack([first, second], axis=axis)
    return jnp.concatenate([first, second], axis=axis)


def body(
    normed,
    router,
    adapter_down,
    adapter_up,
    shared_gate_up,
    shared_down,
    expert_gate_up,
    expert_down,
    lengths,
    adapter_ids,
    routes,
):
    tok_rows = normed.shape[0]
    feat_local = normed.shape[1]
    top_count = routes.shape[1]
    req_count = lax.axis_size("req")
    blk_count = lax.axis_size("blk")
    expert_count = req_count * expert_gate_up.shape[0]
    most_rows = (
        tok_rows * top_count + expert_count - 1
    ) // expert_count + tok_rows * top_count // (12 * expert_count)
    part_rows = -(-most_rows // blk_count)
    most_rows = part_rows * blk_count
    hidden_width = expert_down.shape[1]

    expert_iota = jnp.arange(expert_count, dtype=jnp.int32)
    has = jnp.zeros((tok_rows, expert_count), jnp.float32)
    for k in range(top_count):
        has = has + (routes[:, k][:, None] == expert_iota[None, :]).astype(jnp.float32)
    tok_iota = jnp.arange(tok_rows, dtype=jnp.int32)
    earlier = (tok_iota[None, :] < tok_iota[:, None]).astype(jnp.bfloat16)
    rank = jnp.dot(earlier, has.astype(jnp.bfloat16), preferred_element_type=jnp.float32)
    rank = jnp.where(has > 0, rank, -1.0).astype(jnp.int32)
    pad_rows = -(-part_rows // 16) * 16
    chunk_count = expert_count * blk_count
    row_iota = jnp.arange(chunk_count * pad_rows, dtype=jnp.int32)
    row_slot = (row_iota // pad_rows) % blk_count * part_rows + row_iota % pad_rows
    row_slot = jnp.where(row_iota % pad_rows < part_rows, row_slot, -2)
    rank_rows = jnp.broadcast_to(
        rank.T[:, None, :], (expert_count, blk_count * pad_rows, tok_rows)
    ).reshape(chunk_count * pad_rows, tok_rows)
    pick = rank_rows == row_slot[:, None]

    send_rows = jnp.dot(
        pick.astype(jnp.bfloat16), normed, preferred_element_type=jnp.float32
    ).astype(jnp.bfloat16)
    both = ("req", "blk")
    received = lax.all_to_all(
        send_rows.reshape(chunk_count, pad_rows, feat_local),
        both,
        split_axis=0,
        concat_axis=0,
        tiled=True,
    )
    rows_in = received.reshape(req_count, blk_count, pad_rows, feat_local)

    weight_gate_up = gather_blk(expert_gate_up[0], 0, stack=True)
    gate_up = jnp.einsum(
        "gcsd,cdf->gsf",
        rows_in,
        weight_gate_up,
        preferred_element_type=jnp.float32,
    )
    hidden = (jax.nn.silu(gate_up[..., :hidden_width]) * gate_up[..., hidden_width:]).astype(
        jnp.bfloat16
    )
    hidden_rows = hidden.reshape(req_count * pad_rows, hidden_width)
    weight_down = gather_blk(expert_down[0], 0, stack=True)
    expert_out = jnp.stack(
        [
            jnp.dot(hidden_rows, weight_down[c], preferred_element_type=jnp.float32)
            .astype(jnp.bfloat16)
            .reshape(req_count, pad_rows, feat_local)
            for c in range(blk_count)
        ],
        axis=1,
    )
    returned = lax.all_to_all(
        expert_out.reshape(req_count * blk_count, pad_rows, feat_local),
        both,
        split_axis=0,
        concat_axis=0,
        tiled=True,
    )

    send_rows, router, adapter_down, normed_late = lax.optimization_barrier(
        (send_rows, router, adapter_down, normed)
    )
    normed_full = gather_blk(normed_late, 1)
    small_w = gather_blk(jnp.concatenate([router, adapter_down], axis=1), 0)
    small = jnp.dot(normed_full, small_w, preferred_element_type=jnp.float32)
    logits = small[:, :expert_count]
    low_all = small[:, expert_count:]
    ends = jnp.cumsum(lengths[0])
    request = jnp.sum((tok_iota[:, None] >= ends[None, :]).astype(jnp.int32), axis=1)
    slots_req = jnp.arange(lengths.shape[1], dtype=jnp.int32)
    adapter_token = jnp.sum(
        jnp.where(request[:, None] == slots_req[None, :], adapter_ids[0][None, :], 0), axis=1
    )
    column_owner = jnp.arange(low_all.shape[1], dtype=jnp.int32) // RANK
    low = jnp.where(column_owner[None, :] == adapter_token[:, None], low_all, 0.0).astype(
        jnp.bfloat16
    )
    delta = jnp.dot(low, adapter_up, preferred_element_type=jnp.float32)
    shared_local = shared_gate_up.shape[2]
    shared_flat = shared_gate_up.reshape(shared_gate_up.shape[0], 2 * shared_local)
    shared_pre = jnp.dot(normed_full, shared_flat, preferred_element_type=jnp.float32)
    shared_hidden = (
        jax.nn.silu(shared_pre[:, :shared_local]) * shared_pre[:, shared_local:]
    ).astype(jnp.bfloat16)
    shared_terms = jnp.dot(shared_hidden, shared_down, preferred_element_type=jnp.float32)
    terms = shared_terms.astype(jnp.bfloat16).reshape(tok_rows, blk_count, feat_local)
    mine = lax.axis_index("blk")
    keep = jnp.where(mine == 0, terms[:, 0], terms[:, 1])
    give = jnp.where(mine == 0, terms[:, 1], terms[:, 0])
    shared_out = (keep + partner(give)).astype(jnp.float32)

    chosen = jnp.where(has > 0, jax.nn.sigmoid(logits), 0.0)
    gate = chosen / jnp.sum(chosen, axis=1, keepdims=True)
    rows_per_expert = blk_count * pad_rows
    rank_cols = jnp.broadcast_to(
        rank[:, :, None], (tok_rows, expert_count, rows_per_expert)
    ).reshape(tok_rows, chunk_count * pad_rows)
    gate_cols = jnp.broadcast_to(
        gate[:, :, None], (tok_rows, expert_count, rows_per_expert)
    ).reshape(tok_rows, chunk_count * pad_rows)
    weights = jnp.where(rank_cols == row_slot[None, :], gate_cols, 0.0)
    weights = with_layout_constraint(weights.astype(jnp.bfloat16), Layout(major_to_minor=(0, 1)))
    weights, base = lax.optimization_barrier((weights, shared_out + 0.5 * delta))
    back = returned.reshape(chunk_count * pad_rows, feat_local)
    routed = jnp.dot(weights, back, preferred_element_type=jnp.float32)
    return (base + routed).astype(jnp.bfloat16)


def solution(mesh):
    return jax.shard_map(
        body,
        mesh=mesh,
        in_specs=(
            P("req", "blk"),
            P("blk", None),
            P("blk", None),
            P(None, "blk"),
            P(None, None, "blk"),
            P("blk", None),
            P("req", "blk", None),
            P("req", None, "blk"),
            P("req", None),
            P("req", None),
            P("req", None),
        ),
        out_specs=P("req", "blk"),
        check_vma=False,
    )
```

```python
import jax
import jax.numpy as jnp
from jax import lax
from jax.sharding import PartitionSpec as P

RANK = 16


def partner(x):
    return lax.ppermute(x, "blk", [(0, 1), (1, 0)])


def gather_blk(x, axis, stack=False):
    other = partner(x)
    mine = lax.axis_index("blk")
    first = jnp.where(mine == 0, x, other)
    second = jnp.where(mine == 0, other, x)
    if stack:
        return jnp.stack([first, second], axis=axis)
    return jnp.concatenate([first, second], axis=axis)


def body(
    normed,
    router,
    adapter_down,
    adapter_up,
    shared_gate_up,
    shared_down,
    expert_gate_up,
    expert_down,
    lengths,
    adapter_ids,
    routes,
):
    tok_rows = normed.shape[0]
    feat_local = normed.shape[1]
    top_count = routes.shape[1]
    req_count = lax.axis_size("req")
    blk_count = lax.axis_size("blk")
    expert_count = req_count * expert_gate_up.shape[0]
    most_rows = (
        tok_rows * top_count + expert_count - 1
    ) // expert_count + tok_rows * top_count // (12 * expert_count)
    part_rows = -(-most_rows // blk_count)
    most_rows = part_rows * blk_count
    hidden_width = expert_down.shape[1]

    expert_iota = jnp.arange(expert_count, dtype=jnp.int32)
    has = jnp.zeros((tok_rows, expert_count), jnp.float32)
    for k in range(top_count):
        has = has + (routes[:, k][:, None] == expert_iota[None, :]).astype(jnp.float32)
    tok_iota = jnp.arange(tok_rows, dtype=jnp.int32)
    earlier = (tok_iota[None, :] < tok_iota[:, None]).astype(jnp.bfloat16)
    rank = jnp.dot(earlier, has.astype(jnp.bfloat16), preferred_element_type=jnp.float32)
    rank = jnp.where(has > 0, rank, -1.0).astype(jnp.int32)
    pad_rows = -(-part_rows // 16) * 16
    chunk_count = expert_count * blk_count
    row_iota = jnp.arange(chunk_count * pad_rows, dtype=jnp.int32)
    row_slot = (row_iota // pad_rows) % blk_count * part_rows + row_iota % pad_rows
    row_slot = jnp.where(row_iota % pad_rows < part_rows, row_slot, -2)
    rank_rows = jnp.broadcast_to(
        rank.T[:, None, :], (expert_count, blk_count * pad_rows, tok_rows)
    ).reshape(chunk_count * pad_rows, tok_rows)
    pick = rank_rows == row_slot[:, None]

    send_rows = jnp.dot(
        pick.astype(jnp.bfloat16), normed, preferred_element_type=jnp.float32
    ).astype(jnp.bfloat16)
    both = ("req", "blk")
    received = lax.all_to_all(
        send_rows.reshape(chunk_count, pad_rows, feat_local),
        both,
        split_axis=0,
        concat_axis=0,
        tiled=True,
    )
    rows_in = received.reshape(req_count, blk_count, pad_rows, feat_local)

    weight_gate_up = gather_blk(expert_gate_up[0], 0, stack=True)
    rows_flat = rows_in.reshape(req_count, blk_count * pad_rows, feat_local)
    gate_up = sum(
        jnp.dot(
            rows_flat[:, c * pad_rows : (c + 1) * pad_rows].reshape(req_count * pad_rows, feat_local),
            weight_gate_up[c],
            preferred_element_type=jnp.float32,
        )
        for c in range(blk_count)
    ).reshape(req_count, pad_rows, 2 * hidden_width)
    hidden = (jax.nn.silu(gate_up[..., :hidden_width]) * gate_up[..., hidden_width:]).astype(
        jnp.bfloat16
    )
    hidden_rows = hidden.reshape(req_count * pad_rows, hidden_width)
    weight_down = gather_blk(expert_down[0], 0, stack=True)
    expert_out = jnp.stack(
        [
            jnp.dot(hidden_rows, weight_down[c], preferred_element_type=jnp.float32)
            .astype(jnp.bfloat16)
            .reshape(req_count, pad_rows, feat_local)
            for c in range(blk_count)
        ],
        axis=1,
    )
    returned = lax.all_to_all(
        expert_out.reshape(req_count * blk_count, pad_rows, feat_local),
        both,
        split_axis=0,
        concat_axis=0,
        tiled=True,
    )

    send_rows, router, adapter_down, normed_late = lax.optimization_barrier(
        (send_rows, router, adapter_down, normed)
    )
    normed_full = gather_blk(normed_late, 1)
    small_w = gather_blk(jnp.concatenate([router, adapter_down], axis=1), 0)
    small = jnp.dot(normed_full, small_w, preferred_element_type=jnp.float32)
    logits = small[:, :expert_count]
    low_all = small[:, expert_count:]
    ends = jnp.cumsum(lengths[0])
    request = jnp.sum((tok_iota[:, None] >= ends[None, :]).astype(jnp.int32), axis=1)
    slots_req = jnp.arange(lengths.shape[1], dtype=jnp.int32)
    adapter_token = jnp.sum(
        jnp.where(request[:, None] == slots_req[None, :], adapter_ids[0][None, :], 0), axis=1
    )
    column_owner = jnp.arange(low_all.shape[1], dtype=jnp.int32) // RANK
    low = jnp.where(column_owner[None, :] == adapter_token[:, None], low_all, 0.0).astype(
        jnp.bfloat16
    )
    delta = jnp.dot(low, adapter_up, preferred_element_type=jnp.float32)
    shared_local = shared_gate_up.shape[2]
    shared_flat = shared_gate_up.reshape(shared_gate_up.shape[0], 2 * shared_local)
    shared_pre = jnp.dot(normed_full, shared_flat, preferred_element_type=jnp.float32)
    shared_hidden = (
        jax.nn.silu(shared_pre[:, :shared_local]) * shared_pre[:, shared_local:]
    ).astype(jnp.bfloat16)
    shared_terms = jnp.dot(shared_hidden, shared_down, preferred_element_type=jnp.float32)
    terms = shared_terms.astype(jnp.bfloat16).reshape(tok_rows, blk_count, feat_local)
    mine = lax.axis_index("blk")
    keep = jnp.where(mine == 0, terms[:, 0], terms[:, 1])
    give = jnp.where(mine == 0, terms[:, 1], terms[:, 0])
    shared_out = (keep + partner(give)).astype(jnp.float32)

    chosen = jnp.where(has > 0, jax.nn.sigmoid(logits), 0.0)
    gate = chosen / jnp.sum(chosen, axis=1, keepdims=True)
    rows_per_expert = blk_count * pad_rows
    rank_cols = jnp.broadcast_to(
        rank[:, :, None], (tok_rows, expert_count, rows_per_expert)
    ).reshape(tok_rows, chunk_count * pad_rows)
    gate_cols = jnp.broadcast_to(
        gate[:, :, None], (tok_rows, expert_count, rows_per_expert)
    ).reshape(tok_rows, chunk_count * pad_rows)
    weights = jnp.where(rank_cols == row_slot[None, :], gate_cols, 0.0)
    weights, base = lax.optimization_barrier(
        (weights.astype(jnp.bfloat16), shared_out + 0.5 * delta)
    )
    back = returned.reshape(chunk_count * pad_rows, feat_local)
    routed = jnp.dot(weights, back, preferred_element_type=jnp.float32)
    return (base + routed).astype(jnp.bfloat16)


def solution(mesh):
    return jax.shard_map(
        body,
        mesh=mesh,
        in_specs=(
            P("req", "blk"),
            P("blk", None),
            P("blk", None),
            P(None, "blk"),
            P(None, None, "blk"),
            P("blk", None),
            P("req", "blk", None),
            P("req", None, "blk"),
            P("req", None),
            P("req", None),
            P("req", None),
        ),
        out_specs=P("req", "blk"),
        check_vma=False,
    )
```

```python
import jax
import jax.numpy as jnp
from jax import lax
from jax.sharding import PartitionSpec as P

RANK = 16


def partner(x):
    return lax.ppermute(x, "blk", [(0, 1), (1, 0)])


def gather_blk(x, axis, stack=False):
    other = partner(x)
    mine = lax.axis_index("blk")
    first = jnp.where(mine == 0, x, other)
    second = jnp.where(mine == 0, other, x)
    if stack:
        return jnp.stack([first, second], axis=axis)
    return jnp.concatenate([first, second], axis=axis)


def body(
    normed,
    router,
    adapter_down,
    adapter_up,
    shared_gate_up,
    shared_down,
    expert_gate_up,
    expert_down,
    lengths,
    adapter_ids,
    routes,
):
    tok_rows = normed.shape[0]
    feat_local = normed.shape[1]
    top_count = routes.shape[1]
    req_count = lax.axis_size("req")
    blk_count = lax.axis_size("blk")
    expert_count = req_count * expert_gate_up.shape[0]
    most_rows = (
        tok_rows * top_count + expert_count - 1
    ) // expert_count + tok_rows * top_count // (12 * expert_count)
    part_rows = -(-most_rows // blk_count)
    most_rows = part_rows * blk_count
    hidden_width = expert_down.shape[1]

    expert_iota = jnp.arange(expert_count, dtype=jnp.int32)
    has = jnp.zeros((tok_rows, expert_count), jnp.float32)
    for k in range(top_count):
        has = has + (routes[:, k][:, None] == expert_iota[None, :]).astype(jnp.float32)
    tok_iota = jnp.arange(tok_rows, dtype=jnp.int32)
    earlier = (tok_iota[None, :] < tok_iota[:, None]).astype(jnp.bfloat16)
    rank = jnp.dot(earlier, has.astype(jnp.bfloat16), preferred_element_type=jnp.float32)
    rank = jnp.where(has > 0, rank, -1.0).astype(jnp.int32)
    pad_rows = -(-part_rows // 16) * 16
    chunk_count = expert_count * blk_count
    row_iota = jnp.arange(chunk_count * pad_rows, dtype=jnp.int32)
    row_slot = (row_iota // pad_rows) % blk_count * part_rows + row_iota % pad_rows
    row_slot = jnp.where(row_iota % pad_rows < part_rows, row_slot, -2)
    rank_rows = jnp.broadcast_to(
        rank.T[:, None, :], (expert_count, blk_count * pad_rows, tok_rows)
    ).reshape(chunk_count * pad_rows, tok_rows)
    weight_gate_up = gather_blk(expert_gate_up[0], 0, stack=True)
    weight_down = gather_blk(expert_down[0], 0, stack=True)
    weight_gate_up, weight_down, rank_rows = lax.optimization_barrier(
        (weight_gate_up, weight_down, rank_rows)
    )
    pick = rank_rows == row_slot[:, None]

    send_rows = jnp.dot(
        pick.astype(jnp.bfloat16), normed, preferred_element_type=jnp.float32
    ).astype(jnp.bfloat16)
    both = ("req", "blk")
    received = lax.all_to_all(
        send_rows.reshape(chunk_count, pad_rows, feat_local),
        both,
        split_axis=0,
        concat_axis=0,
        tiled=True,
    )
    rows_in = received.reshape(req_count, blk_count, pad_rows, feat_local)


    gate_up = jnp.einsum(
        "gcsd,cdf->gsf",
        rows_in,
        weight_gate_up,
        preferred_element_type=jnp.float32,
    )
    hidden = (jax.nn.silu(gate_up[..., :hidden_width]) * gate_up[..., hidden_width:]).astype(
        jnp.bfloat16
    )
    hidden_rows = hidden.reshape(req_count * pad_rows, hidden_width)
    expert_out = jnp.stack(
        [
            jnp.dot(hidden_rows, weight_down[c], preferred_element_type=jnp.float32)
            .astype(jnp.bfloat16)
            .reshape(req_count, pad_rows, feat_local)
            for c in range(blk_count)
        ],
        axis=1,
    )
    returned = lax.all_to_all(
        expert_out.reshape(req_count * blk_count, pad_rows, feat_local),
        both,
        split_axis=0,
        concat_axis=0,
        tiled=True,
    )

    send_rows, router, adapter_down, normed_late = lax.optimization_barrier(
        (send_rows, router, adapter_down, normed)
    )
    normed_full = gather_blk(normed_late, 1)
    small_w = gather_blk(jnp.concatenate([router, adapter_down], axis=1), 0)
    small = jnp.dot(normed_full, small_w, preferred_element_type=jnp.float32)
    logits = small[:, :expert_count]
    low_all = small[:, expert_count:]
    ends = jnp.cumsum(lengths[0])
    request = jnp.sum((tok_iota[:, None] >= ends[None, :]).astype(jnp.int32), axis=1)
    slots_req = jnp.arange(lengths.shape[1], dtype=jnp.int32)
    adapter_token = jnp.sum(
        jnp.where(request[:, None] == slots_req[None, :], adapter_ids[0][None, :], 0), axis=1
    )
    column_owner = jnp.arange(low_all.shape[1], dtype=jnp.int32) // RANK
    low = jnp.where(column_owner[None, :] == adapter_token[:, None], low_all, 0.0).astype(
        jnp.bfloat16
    )
    delta = jnp.dot(low, adapter_up, preferred_element_type=jnp.float32)
    shared_local = shared_gate_up.shape[2]
    shared_flat = shared_gate_up.reshape(shared_gate_up.shape[0], 2 * shared_local)
    shared_pre = jnp.dot(normed_full, shared_flat, preferred_element_type=jnp.float32)
    shared_hidden = (
        jax.nn.silu(shared_pre[:, :shared_local]) * shared_pre[:, shared_local:]
    ).astype(jnp.bfloat16)
    shared_terms = jnp.dot(shared_hidden, shared_down, preferred_element_type=jnp.float32)
    terms = shared_terms.astype(jnp.bfloat16).reshape(tok_rows, blk_count, feat_local)
    mine = lax.axis_index("blk")
    keep = jnp.where(mine == 0, terms[:, 0], terms[:, 1])
    give = jnp.where(mine == 0, terms[:, 1], terms[:, 0])
    shared_out = (keep + partner(give)).astype(jnp.float32)

    chosen = jnp.where(has > 0, jax.nn.sigmoid(logits), 0.0)
    gate = chosen / jnp.sum(chosen, axis=1, keepdims=True)
    rows_per_expert = blk_count * pad_rows
    rank_cols = jnp.broadcast_to(
        rank[:, :, None], (tok_rows, expert_count, rows_per_expert)
    ).reshape(tok_rows, chunk_count * pad_rows)
    gate_cols = jnp.broadcast_to(
        gate[:, :, None], (tok_rows, expert_count, rows_per_expert)
    ).reshape(tok_rows, chunk_count * pad_rows)
    weights = jnp.where(rank_cols == row_slot[None, :], gate_cols, 0.0)
    weights, base = lax.optimization_barrier(
        (weights.astype(jnp.bfloat16), shared_out + 0.5 * delta)
    )
    back = returned.reshape(chunk_count * pad_rows, feat_local)
    routed = jnp.dot(weights, back, preferred_element_type=jnp.float32)
    return (base + routed).astype(jnp.bfloat16)


def solution(mesh):
    return jax.shard_map(
        body,
        mesh=mesh,
        in_specs=(
            P("req", "blk"),
            P("blk", None),
            P("blk", None),
            P(None, "blk"),
            P(None, None, "blk"),
            P("blk", None),
            P("req", "blk", None),
            P("req", None, "blk"),
            P("req", None),
            P("req", None),
            P("req", None),
        ),
        out_specs=P("req", "blk"),
        check_vma=False,
    )
```
